256 devices in a mesh: dp: 16 (over z, core), expert: 16 (over x, y).
Axes of the slice: x: 4, y: 4, z: 8, core: 2. Of those that a mesh axis runs over, the one named last changes fastest.
Arguments:
- hidden_in: bfloat16 [16384, 2048], P(('dp', 'expert')), parts along dimension 0, may hold values from -6 to 6
- route_ids: int32 [16384, 8], P(('dp', 'expert')), parts along dimension 0, may hold values from 0 to 15, all different within a row; in each aligned block of 64 rows (0 to 63, 64 to 127, ...) at most 64 rows name the same one
- gates: float32 [16384, 8], P(('dp', 'expert')), parts along dimension 0, may hold values from 0.05 to 1
- w_in: bfloat16 [16, 2048, 1536], P('expert'), may hold values from -0.125 to 0.125
- w_out: bfloat16 [16, 768, 2048], P('expert'), may hold values from -0.21875 to 0.21875
Outputs:
- combined: bfloat16 [16384, 2048], P(('dp', 'expert')), parts along dimension 0
The draws below stay inside these ranges and needn't reach their ends.
There are 16 independent parts, one for each index of `dp`. The reference program is written for one: setup_inputs(seed, part) draws one part's arguments, and reference() takes and returns one part's arrays. A program takes and returns all parts, laid end to end along the dimension named above; an argument that names none is the same for every part. Nothing has to cross between parts.
Inputs may be any that keep to these rules, and one draw needn't show every extreme that they name: `route_ids`: each row names 8 different experts. Among the rows of one device (aligned blocks of 64 rows) no expert is named by more than 64 rows, and in every draw some expert is named by exactly 64 rows of some block.
All inputs are finite; a program needn't handle non-finite values.
Results may differ from the reference program's by a relative error of at most 0.0085.
Values may be sent and summed in bfloat16 or wider, within the bound.
No kernel may reach another device: no remote copies, remote signals or barrier semaphores. Data moves between devices by JAX's collectives and lax.ppermute only.
A program may use at most 64 MiB of HBM per device.

```python
import math
import jax
import jax.numpy as jnp
import numpy as np
from jax import lax

D = 2048
FF = 768
ROWS_DEV = 64
EXPERTS = 16
TOP = 8
CAP = 64
ROWS = 1024


def block_levels(own_key, shape, shards, least, top_value):
    def one(dim, blocks):
        heights = jax.random.uniform(jax.random.fold_in(jax.random.fold_in(own_key, 6), dim), (blocks,), jnp.float32, least / len(shards), top_value / len(shards))
        return jnp.repeat(jnp.exp(heights), shape[dim] // blocks).reshape((-1,) + (1,) * (len(shape) - dim - 1))

    factor_of = one(*shards[0])
    for cut in shards[1:]:
        factor_of = factor_of * one(*cut)
    return factor_of


def shared_out(rng, own, number, rows, count, top, limit, skew):
    order = jax.random.permutation(rng, count)
    packed, ordinary = portions_of(count, rows * top, limit, skew, True), portions_of(count, rows * top, limit, skew, False)
    places = jnp.arange(count)

    def named(sizes, offset_by):
        used = int((sizes > 0).sum())
        fixed = max(1, used // 4)
        shifted = fixed + (places - fixed + offset_by * (used - fixed)) % max(1, count - fixed)
        return jnp.zeros((count,), jnp.int32).at[order[jnp.where(places < fixed, places, shifted)]].set(jnp.asarray(sizes, jnp.int32))

    sizes = jnp.where(number % 4 == 0, named(packed, number // 4), named(ordinary, number - number // 4 - 1))
    mixed = jax.random.permutation(jax.random.fold_in(own, 3), count)
    giver, sink = mixed[0:count // 2 * 2:2], mixed[1:count // 2 * 2:2]
    slack = jnp.minimum(sizes[giver] - 1, limit - sizes[sink]) // 2
    slack = jnp.where((giver == order[0]) | (sink == order[0]) | (sizes[sink] == 0), 0, jnp.maximum(slack, 0))
    shifted = jax.random.randint(jax.random.fold_in(own, 4), (count // 2,), 0, 1 << 20) % (slack + 1)
    sizes = sizes.at[giver].add(-shifted).at[sink].add(shifted)
    members = jnp.searchsorted(jnp.cumsum(sizes), jnp.arange(rows * top), side="right").astype(jnp.int32)
    grid = members.reshape(top, rows).T
    grid = grid[jax.random.permutation(jax.random.fold_in(own, 1), rows)]
    offset_by = jax.random.randint(jax.random.fold_in(own, 2), (rows, 1), 0, top)
    return jnp.take_along_axis(grid, (jnp.arange(top)[None, :] + offset_by) % top, axis=1)


def portions_of(number_of, total, reach, slope, full):
    loads = [(1 << 20) // math.isqrt(standing ** slope) + 1 for standing in range(1, number_of + 1)]
    largest = reach if full else min(reach, max(-(-total // number_of), total * loads[0] // sum(loads)))
    least = 1 if total - largest >= number_of - 1 else 0
    given, rest = [largest] + [least] * (number_of - 1), total - largest - least * (number_of - 1)
    while rest > 0:
        free = [i for i in range(1, number_of) if given[i] < largest] or [i for i in range(1, number_of) if given[i] < reach]
        mass, left = sum([loads[i] for i in free]), rest
        for i in free:
            more = min(reach - given[i], max(1, left * loads[i] // mass), rest)
            given[i] = given[i] + more
            rest = rest - more
    return np.array(given)


def noise(stream_key, shape, scale, most, pieces=(), kind=jnp.bfloat16):
    array = jax.random.normal(stream_key, shape, jnp.float32) * scale
    if len(pieces) > 0:
        array = block_levels(stream_key, shape, pieces, -0.22, 0.18) * array
    return jnp.clip(array, min=-most, max=most).astype(kind)


def setup_inputs(seed: int = 0, part: int = 0) -> dict:
    keys = jax.random.split(jax.random.key(seed), 6)
    part_splits = jax.random.split(jax.random.fold_in(keys[5], part), 6)
    hidden_in = noise(part_splits[0], (ROWS, D), 1.0, 6.0, ((0, 16),))
    route_ids_keys = jax.random.split(jax.random.fold_in(part_splits[1], 1), ROWS // ROWS_DEV)
    route_ids_turns = jax.random.permutation(jax.random.fold_in(part_splits[1], 3), ROWS // ROWS_DEV)
    route_ids = jax.vmap(lambda own, number: shared_out(jax.random.fold_in(part_splits[1], 2), own, number, ROWS_DEV, EXPERTS, TOP, CAP, 2))(route_ids_keys, route_ids_turns).reshape((ROWS, TOP))
    gates = jnp.clip(jnp.exp(math.log(1.0) - 2.9957323 * jax.random.uniform(part_splits[2], (ROWS, TOP), jnp.float32) ** block_levels(part_splits[2], (ROWS, TOP), ((0, 16),), -0.2, 0.2)), 0.05, 1.0)
    w_in = noise(keys[3], (EXPERTS, D, 2 * FF), D ** -0.5, 0.125, ((0, 16),))
    w_out = noise(keys[4], (EXPERTS, FF, D), FF ** -0.5, 0.21875, ((0, 16),))
    return dict(hidden_in=hidden_in, route_ids=route_ids, gates=gates, w_in=w_in, w_out=w_out)


def reference(hidden_in, route_ids, gates, w_in, w_out):
    def one_expert(carry, expert_id):
        weight_row = jnp.sum(jnp.where(route_ids == expert_id, gates, jnp.float32(0.0)), axis=1)
        projected = jnp.dot(hidden_in, w_in[expert_id], preferred_element_type=jnp.float32)
        inner = (jax.nn.silu(projected[:, :FF]) * projected[:, FF:]).astype(jnp.bfloat16)
        result = jnp.dot(inner, w_out[expert_id], preferred_element_type=jnp.float32).astype(jnp.bfloat16)
        return carry + weight_row[:, None] * result.astype(jnp.float32), None

    start = jnp.zeros((hidden_in.shape[0], D), jnp.float32)
    total, unused = lax.scan(one_expert, start, jnp.arange(EXPERTS, dtype=jnp.int32))
    return total.astype(jnp.bfloat16)
```

```python
import jax
import jax.numpy as jnp
from jax import lax
from jax.sharding import PartitionSpec as P


def body(hidden_in, route_ids, gates, w_in, w_out):
    groups = lax.axis_size("expert")
    me = lax.axis_index("expert")
    half = w_out.shape[1]
    experts = jnp.arange(groups, dtype=jnp.int32)
    dense = jnp.sum(
        jnp.where(route_ids[:, :, None] == experts, gates[:, :, None], jnp.float32(0.0)), axis=1
    )
    rows = lax.all_gather(hidden_in, "expert", axis=0, tiled=True)
    weights = lax.all_gather(dense, "expert", axis=0, tiled=True)
    mine = jnp.sum(jnp.where(experts[None, :] == me, weights, jnp.float32(0.0)), axis=1)
    projected = jnp.dot(rows, w_in[0], preferred_element_type=jnp.float32)
    inner = (jax.nn.silu(projected[:, :half]) * projected[:, half:]).astype(jnp.bfloat16)
    produced = jnp.dot(inner, w_out[0], preferred_element_type=jnp.float32).astype(jnp.bfloat16)
    weighted = (mine[:, None] * produced.astype(jnp.float32)).astype(jnp.bfloat16)
    total = lax.psum_scatter(weighted, "expert", scatter_dimension=0, tiled=True)
    return total


def solution(mesh):
    placed = (
        P(("dp", "expert"), None),
        P(("dp", "expert"), None),
        P(("dp", "expert"), None),
        P("expert", None, None),
        P("expert", None, None),
    )
    return jax.shard_map(
        body, mesh=mesh, in_specs=placed, out_specs=P(("dp", "expert"), None), check_vma=False
    )
```

```python
import jax
import jax.numpy as jnp
from jax import lax
from jax.sharding import PartitionSpec as P

SIDE = 4


def shift(tree, axis, step):
    pairs = []
    for x in range(SIDE):
        for y in range(SIDE):
            if axis == "x":
                pairs.append((x * SIDE + y, ((x + step) % SIDE) * SIDE + y))
            else:
                pairs.append((x * SIDE + y, x * SIDE + (y + step) % SIDE))
    return lax.ppermute(tree, "expert", pairs)


def gather_ring(tree, axis):
    right = shift(tree, axis, -1)
    left = shift(tree, axis, 1)
    cut = jax.tree.leaves(tree)[0].shape[0] // 2
    far_a = shift(jax.tree.map(lambda v: v[:cut], left), axis, 1)
    far_b = shift(jax.tree.map(lambda v: v[cut:], right), axis, -1)
    far = jax.tree.map(lambda a, b: jnp.concatenate([a, b], axis=0), far_a, far_b)
    return jax.tree.map(lambda *vs: jnp.concatenate(vs, axis=0), tree, right, far, left)


def scatter_ring(parts, axis):
    cut = parts.shape[1] // 2
    got_a = shift(parts[2, :cut].astype(jnp.bfloat16), axis, 1)
    got_b = shift(parts[2, cut:].astype(jnp.bfloat16), axis, -1)
    to_right = jnp.concatenate([parts[1, :cut] + got_a.astype(jnp.float32), parts[1, cut:]], axis=0)
    to_left = jnp.concatenate([parts[3, :cut], parts[3, cut:] + got_b.astype(jnp.float32)], axis=0)
    from_left = shift(to_right.astype(jnp.bfloat16), axis, 1)
    from_right = shift(to_left.astype(jnp.bfloat16), axis, -1)
    return parts[0] + from_left.astype(jnp.float32) + from_right.astype(jnp.float32)


def expert_rows(rows, table, me, w_in, w_out):
    half = w_out.shape[0]
    experts = jnp.arange(table.shape[1], dtype=jnp.int32)
    mine = jnp.sum(jnp.where(experts[None, :] == me, table, jnp.float32(0.0)), axis=1)
    projected = jnp.dot(rows, w_in, preferred_element_type=jnp.float32)
    inner = (jax.nn.silu(projected[:, :half]) * projected[:, half:]).astype(jnp.bfloat16)
    produced = jnp.dot(inner, w_out, preferred_element_type=jnp.float32).astype(jnp.bfloat16)
    return mine[:, None] * produced.astype(jnp.float32)


def body(hidden_in, route_ids, gates, w_in, w_out):
    assert lax.axis_size("expert") == SIDE * SIDE
    me = lax.axis_index("expert")
    width = hidden_in.shape[1]
    experts = jnp.arange(SIDE * SIDE, dtype=jnp.int32)
    table = jnp.sum(
        jnp.where(route_ids[:, :, None] == experts, gates[:, :, None], jnp.float32(0.0)), axis=1
    )
    split = hidden_in.shape[0] // 2
    orders = (("x", "y"), ("y", "x"))
    gathered = []
    for i, (first, second) in enumerate(orders):
        own = (hidden_in[i * split:(i + 1) * split], table[i * split:(i + 1) * split])
        gathered.append(gather_ring(gather_ring(own, first), second))
    rows = jnp.concatenate([g[0] for g in gathered], axis=0)
    tables = jnp.concatenate([g[1] for g in gathered], axis=0)
    weighted = expert_rows(rows, tables, me, w_in[0], w_out[0])
    outs = []
    for i, (first, second) in enumerate(orders):
        part = weighted[i * 16 * split:(i + 1) * 16 * split].reshape(SIDE, SIDE * split, width)
        stage = scatter_ring(part, second).reshape(SIDE, split, width)
        outs.append(scatter_ring(stage, first))
    return jnp.concatenate(outs, axis=0).astype(jnp.bfloat16)


def solution(mesh):
    placed = (
        P(("dp", "expert"), None),
        P(("dp", "expert"), None),
        P(("dp", "expert"), None),
        P("expert", None, None),
        P("expert", None, None),
    )
    return jax.shard_map(
        body, mesh=mesh, in_specs=placed, out_specs=P(("dp", "expert"), None), check_vma=False
    )
```

```python
import jax
import jax.numpy as jnp
import numpy as np
from jax import lax
from jax.sharding import Mesh
from jax.sharding import PartitionSpec as P

SIDE = 4
PAD = 128


def spread(block, axis):
    copies = jnp.broadcast_to(block[None], (SIDE,) + block.shape)
    return lax.all_to_all(copies, axis, 0, 0, tiled=False)


def collect(parts, axis):
    moved = lax.all_to_all(parts.astype(jnp.bfloat16), axis, 0, 0, tiled=False)
    return jnp.sum(moved.astype(jnp.float32), axis=0)


def body(hidden_in, route_ids, gates, w_in, w_out):
    me = lax.axis_index("ex") * SIDE + lax.axis_index("ey")
    count, width = hidden_in.shape
    half = w_out.shape[1]
    experts = jnp.arange(SIDE * SIDE, dtype=jnp.int32)
    table = jnp.sum(
        jnp.where(route_ids[:, :, None] == experts, gates[:, :, None], jnp.float32(0.0)), axis=1
    )
    high = table.astype(jnp.bfloat16)
    low = (table - high.astype(jnp.float32)).astype(jnp.bfloat16)
    extra = jnp.zeros((count, PAD - 2 * SIDE * SIDE), jnp.bfloat16)
    payload = jnp.concatenate([hidden_in, high, low, extra], axis=1)
    split = count // 2
    orders = (("ex", "ey"), ("ey", "ex"))
    gathered = []
    for i, (first, second) in enumerate(orders):
        own = payload[i * split:(i + 1) * split]
        stage = spread(own, first).reshape(SIDE * split, -1)
        gathered.append(spread(stage, second).reshape(SIDE * SIDE * split, -1))
    rows = jnp.concatenate(gathered, axis=0)
    picked = (experts == me)[None, :]
    got_high = rows[:, width:width + SIDE * SIDE].astype(jnp.float32)
    got_low = rows[:, width + SIDE * SIDE:width + 2 * SIDE * SIDE].astype(jnp.float32)
    mine = jnp.sum(jnp.where(picked, got_high + got_low, jnp.float32(0.0)), axis=1)
    projected = jnp.dot(rows[:, :width], w_in[0], preferred_element_type=jnp.float32)
    inner = (jax.nn.silu(projected[:, :half]) * projected[:, half:]).astype(jnp.bfloat16)
    produced = jnp.dot(inner, w_out[0], preferred_element_type=jnp.float32).astype(jnp.bfloat16)
    weighted = mine[:, None] * produced.astype(jnp.float32)
    outs = []
    for i, (first, second) in enumerate(orders):
        part = weighted[i * SIDE * SIDE * split:(i + 1) * SIDE * SIDE * split]
        stage = collect(part.reshape(SIDE, SIDE * split, width), second)
        outs.append(collect(stage.reshape(SIDE, split, width), first))
    return jnp.concatenate(outs, axis=0).astype(jnp.bfloat16)


def solution(mesh):
    grid = Mesh(mesh.devices.reshape(mesh.shape["dp"], SIDE, SIDE), ("dp", "ex", "ey"))
    rows = P(("dp", "ex", "ey"), None)
    placed = (rows, rows, rows, P(("ex", "ey"), None, None), P(("ex", "ey"), None, None))
    return jax.shard_map(body, mesh=grid, in_specs=placed, out_specs=rows, check_vma=False)
```

```python
import jax
import jax.numpy as jnp
from jax import lax
from jax.sharding import PartitionSpec as P

CHUNKS = 2


def slot_ranks(choices, count):
    flat = choices.reshape(-1)
    length = flat.shape[0]
    onehot = (flat[:, None] == jnp.arange(count, dtype=jnp.int32)).astype(jnp.bfloat16)
    lower = (
        jnp.arange(length, dtype=jnp.int32)[:, None] > jnp.arange(length, dtype=jnp.int32)[None, :]
    ).astype(jnp.bfloat16)
    ranks = jnp.dot(lower, onehot, preferred_element_type=jnp.float32)
    picked = jnp.sum(ranks * onehot.astype(jnp.float32), axis=-1)
    return picked.astype(jnp.int32).reshape(choices.shape)


def body(hidden_in, route_ids, gates, w_in, w_out):
    groups = lax.axis_size("expert")
    rows_here, width = hidden_in.shape
    half = w_out.shape[1]
    capacity = rows_here
    per_chunk = capacity // CHUNKS
    slots_all = capacity * groups
    rank = slot_ranks(route_ids, groups)
    chunk = rank // per_chunk
    slot = chunk * (groups * per_chunk) + route_ids * per_chunk + rank % per_chunk
    hit = slot[:, :, None] == jnp.arange(slots_all, dtype=jnp.int32)
    placement = jnp.sum(hit.astype(jnp.bfloat16), axis=1)
    weighting = jnp.sum(jnp.where(hit, gates[:, :, None], jnp.float32(0.0)), axis=1)
    high = weighting.astype(jnp.bfloat16)
    low = (weighting - high.astype(jnp.float32)).astype(jnp.bfloat16)
    outgoing = jnp.dot(placement.T, hidden_in, preferred_element_type=jnp.float32)
    outgoing = outgoing.astype(jnp.bfloat16).reshape(CHUNKS, groups, per_chunk, width)
    total = jnp.zeros((rows_here, width), jnp.float32)
    for c in range(CHUNKS):
        arrived = lax.all_to_all(outgoing[c], "expert", 0, 0, tiled=False)
        projected = jnp.dot(
            arrived.reshape(groups * per_chunk, width), w_in[0], preferred_element_type=jnp.float32
        )
        inner = (jax.nn.silu(projected[:, :half]) * projected[:, half:]).astype(jnp.bfloat16)
        produced = jnp.dot(inner, w_out[0], preferred_element_type=jnp.float32).astype(jnp.bfloat16)
        returned = lax.all_to_all(
            produced.reshape(groups, per_chunk, width), "expert", 0, 0, tiled=False
        ).reshape(groups * per_chunk, width)
        cols = slice(c * groups * per_chunk, (c + 1) * groups * per_chunk)
        total = total + jnp.dot(high[:, cols], returned, preferred_element_type=jnp.float32)
        total = total + jnp.dot(low[:, cols], returned, preferred_element_type=jnp.float32)
    return total.astype(jnp.bfloat16)


def solution(mesh):
    placed = (
        P(("dp", "expert"), None),
        P(("dp", "expert"), None),
        P(("dp", "expert"), None),
        P("expert", None, None),
        P("expert", None, None),
    )
    return jax.shard_map(
        body, mesh=mesh, in_specs=placed, out_specs=P(("dp", "expert"), None), check_vma=False
    )
```

```python
import jax
import jax.numpy as jnp
from jax import lax
from jax.sharding import PartitionSpec as P

CHUNKS = 1


def slot_ranks(choices, count):
    flat = choices.reshape(-1)
    length = flat.shape[0]
    onehot = (flat[:, None] == jnp.arange(count, dtype=jnp.int32)).astype(jnp.bfloat16)
    lower = (
        jnp.arange(length, dtype=jnp.int32)[:, None] > jnp.arange(length, dtype=jnp.int32)[None, :]
    ).astype(jnp.bfloat16)
    ranks = jnp.dot(lower, onehot, preferred_element_type=jnp.float32)
    picked = jnp.sum(ranks * onehot.astype(jnp.float32), axis=-1)
    return picked.astype(jnp.int32).reshape(choices.shape)


def body(hidden_in, route_ids, gates, w_in, w_out):
    groups = lax.axis_size("expert")
    rows_here, width = hidden_in.shape
    half = w_out.shape[1]
    capacity = rows_here
    per_chunk = capacity // CHUNKS
    slots_all = capacity * groups
    rank = slot_ranks(route_ids, groups)
    chunk = rank // per_chunk
    slot = chunk * (groups * per_chunk) + route_ids * per_chunk + rank % per_chunk
    hit = slot[:, :, None] == jnp.arange(slots_all, dtype=jnp.int32)
    placement = jnp.sum(hit.astype(jnp.bfloat16), axis=1)
    weighting = jnp.sum(jnp.where(hit, gates[:, :, None], jnp.float32(0.0)), axis=1)
    outgoing = jnp.dot(placement.T, hidden_in, preferred_element_type=jnp.float32)
    outgoing = outgoing.astype(jnp.bfloat16).reshape(CHUNKS, groups, per_chunk, width)
    total = jnp.zeros((rows_here, width), jnp.float32)
    for c in range(CHUNKS):
        arrived = lax.all_to_all(outgoing[c], "expert", 0, 0, tiled=False)
        projected = jnp.dot(
            arrived.reshape(groups * per_chunk, width), w_in[0], preferred_element_type=jnp.float32
        )
        inner = (jax.nn.silu(projected[:, :half]) * projected[:, half:]).astype(jnp.bfloat16)
        produced = jnp.dot(inner, w_out[0], preferred_element_type=jnp.float32).astype(jnp.bfloat16)
        returned = lax.all_to_all(
            produced.reshape(groups, per_chunk, width), "expert", 0, 0, tiled=False
        ).reshape(groups * per_chunk, width)
        cols = slice(c * groups * per_chunk, (c + 1) * groups * per_chunk)
        total = total + jnp.dot(
            weighting[:, cols], returned.astype(jnp.float32), precision=lax.Precision.HIGHEST
        )
    return total.astype(jnp.bfloat16)


def solution(mesh):
    placed = (
        P(("dp", "expert"), None),
        P(("dp", "expert"), None),
        P(("dp", "expert"), None),
        P("expert", None, None),
        P("expert", None, None),
    )
    return jax.shard_map(
        body, mesh=mesh, in_specs=placed, out_specs=P(("dp", "expert"), None), check_vma=False
    )
```

```python
import jax
import jax.numpy as jnp
from jax import lax
from jax.sharding import PartitionSpec as P

SIDE = 4
PAD = 128


def shift(tree, axis, step):
    pairs = []
    for x in range(SIDE):
        for y in range(SIDE):
            if axis == "x":
                pairs.append((x * SIDE + y, ((x + step) % SIDE) * SIDE + y))
            else:
                pairs.append((x * SIDE + y, x * SIDE + (y + step) % SIDE))
    return lax.ppermute(tree, "expert", pairs)


def gather_ring(tree, axis):
    right = shift(tree, axis, -1)
    left = shift(tree, axis, 1)
    cut = jax.tree.leaves(tree)[0].shape[0] // 2
    far_a = shift(jax.tree.map(lambda v: v[:cut], left), axis, 1)
    far_b = shift(jax.tree.map(lambda v: v[cut:], right), axis, -1)
    far = jax.tree.map(lambda a, b: jnp.concatenate([a, b], axis=0), far_a, far_b)
    return jax.tree.map(lambda *vs: jnp.concatenate(vs, axis=0), tree, right, far, left)


def scatter_ring(parts, axis):
    cut = parts.shape[1] // 2
    got_a = shift(parts[2, :cut].astype(jnp.bfloat16), axis, 1)
    got_b = shift(parts[2, cut:].astype(jnp.bfloat16), axis, -1)
    to_right = jnp.concatenate([parts[1, :cut] + got_a.astype(jnp.float32), parts[1, cut:]], axis=0)
    to_left = jnp.concatenate([parts[3, :cut], parts[3, cut:] + got_b.astype(jnp.float32)], axis=0)
    from_left = shift(to_right.astype(jnp.bfloat16), axis, 1)
    from_right = shift(to_left.astype(jnp.bfloat16), axis, -1)
    return parts[0] + from_left.astype(jnp.float32) + from_right.astype(jnp.float32)


def expert_rows(rows, me, width, w_in, w_out):
    half = w_out.shape[0]
    count = SIDE * SIDE
    experts = jnp.arange(count, dtype=jnp.int32)
    high = rows[:, width:width + count].astype(jnp.float32)
    low = rows[:, width + count:width + 2 * count].astype(jnp.float32)
    mine = jnp.sum(jnp.where(experts[None, :] == me, high + low, jnp.float32(0.0)), axis=1)
    projected = jnp.dot(rows[:, :width], w_in, preferred_element_type=jnp.float32)
    inner = (jax.nn.silu(projected[:, :half]) * projected[:, half:]).astype(jnp.bfloat16)
    produced = jnp.dot(inner, w_out, preferred_element_type=jnp.float32).astype(jnp.bfloat16)
    return mine[:, None] * produced.astype(jnp.float32)


def body(hidden_in, route_ids, gates, w_in, w_out):
    assert lax.axis_size("expert") == SIDE * SIDE
    me = lax.axis_index("expert")
    count, width = hidden_in.shape
    experts = jnp.arange(SIDE * SIDE, dtype=jnp.int32)
    table = jnp.sum(
        jnp.where(route_ids[:, :, None] == experts, gates[:, :, None], jnp.float32(0.0)), axis=1
    )
    high = table.astype(jnp.bfloat16)
    low = (table - high.astype(jnp.float32)).astype(jnp.bfloat16)
    extra = jnp.zeros((count, PAD - 2 * SIDE * SIDE), jnp.bfloat16)
    payload = jnp.concatenate([hidden_in, high, low, extra], axis=1)
    split = count // 2
    orders = (("x", "y"), ("y", "x"))
    gathered = []
    for i, (first, second) in enumerate(orders):
        own = payload[i * split:(i + 1) * split]
        gathered.append(gather_ring(gather_ring(own, first), second))
    rows = jnp.concatenate(gathered, axis=0)
    weighted = expert_rows(rows, me, width, w_in[0], w_out[0])
    outs = []
    for i, (first, second) in enumerate(orders):
        part = weighted[i * 16 * split:(i + 1) * 16 * split].reshape(SIDE, SIDE * split, width)
        stage = scatter_ring(part, second).reshape(SIDE, split, width)
        outs.append(scatter_ring(stage, first))
    return jnp.concatenate(outs, axis=0).astype(jnp.bfloat16)


def solution(mesh):
    placed = (
        P(("dp", "expert"), None),
        P(("dp", "expert"), None),
        P(("dp", "expert"), None),
        P("expert", None, None),
        P("expert", None, None),
    )
    return jax.shard_map(
        body, mesh=mesh, in_specs=placed, out_specs=P(("dp", "expert"), None), check_vma=False
    )
```

```python
import jax
import jax.numpy as jnp
from jax import lax
from jax.sharding import Mesh
from jax.sharding import PartitionSpec as P

SIDE = 4
PAD = 128


def body(hidden_in, route_ids, gates, w_in, w_out):
    me = lax.axis_index("ex") * SIDE + lax.axis_index("ey")
    count, width = hidden_in.shape
    half = w_out.shape[1]
    experts = jnp.arange(SIDE * SIDE, dtype=jnp.int32)
    table = jnp.sum(
        jnp.where(route_ids[:, :, None] == experts, gates[:, :, None], jnp.float32(0.0)), axis=1
    )
    high = table.astype(jnp.bfloat16)
    low = (table - high.astype(jnp.float32)).astype(jnp.bfloat16)
    extra = jnp.zeros((count, PAD - 2 * SIDE * SIDE), jnp.bfloat16)
    payload = jnp.concatenate([hidden_in, high, low, extra], axis=1)
    stage = lax.all_gather(payload, "ey", axis=0, tiled=True)
    rows = lax.all_gather(stage, "ex", axis=0, tiled=True)
    picked = (experts == me)[None, :]
    got_high = rows[:, width:width + SIDE * SIDE].astype(jnp.float32)
    got_low = rows[:, width + SIDE * SIDE:width + 2 * SIDE * SIDE].astype(jnp.float32)
    mine = jnp.sum(jnp.where(picked, got_high + got_low, jnp.float32(0.0)), axis=1)
    projected = jnp.dot(rows[:, :width], w_in[0], preferred_element_type=jnp.float32)
    inner = (jax.nn.silu(projected[:, :half]) * projected[:, half:]).astype(jnp.bfloat16)
    produced = jnp.dot(inner, w_out[0], preferred_element_type=jnp.float32).astype(jnp.bfloat16)
    weighted = (mine[:, None] * produced.astype(jnp.float32)).astype(jnp.bfloat16)
    part = lax.psum_scatter(weighted, "ex", scatter_dimension=0, tiled=True)
    return lax.psum_scatter(part, "ey", scatter_dimension=0, tiled=True)


def solution(mesh):
    grid = Mesh(mesh.devices.reshape(mesh.shape["dp"], SIDE, SIDE), ("dp", "ex", "ey"))
    rows = P(("dp", "ex", "ey"), None)
    placed = (rows, rows, rows, P(("ex", "ey"), None, None), P(("ex", "ey"), None, None))
    return jax.shard_map(body, mesh=grid, in_specs=placed, out_specs=rows, check_vma=False)
```

```python
import jax
import jax.numpy as jnp
from jax import lax
from jax.sharding import PartitionSpec as P

SIDE = 4
PAD = 128


def shift(tree, stage, step):
    parts = lax.axis_size("dp")
    pairs = []
    for d in range(parts):
        along_x = (d + stage) % 2 == 0
        for x in range(SIDE):
            for y in range(SIDE):
                if along_x:
                    target = ((x + step) % SIDE) * SIDE + y
                else:
                    target = x * SIDE + (y + step) % SIDE
                pairs.append((d * SIDE * SIDE + x * SIDE + y, d * SIDE * SIDE + target))
    return lax.ppermute(tree, ("dp", "expert"), pairs)


def gather_ring(tree, axis):
    right = shift(tree, axis, -1)
    left = shift(tree, axis, 1)
    cut = jax.tree.leaves(tree)[0].shape[0] // 2
    far_a = shift(jax.tree.map(lambda v: v[:cut], left), axis, 1)
    far_b = shift(jax.tree.map(lambda v: v[cut:], right), axis, -1)
    far = jax.tree.map(lambda a, b: jnp.concatenate([a, b], axis=0), far_a, far_b)
    return jax.tree.map(lambda *vs: jnp.concatenate(vs, axis=0), tree, right, far, left)


def scatter_ring(parts, axis):
    cut = parts.shape[1] // 2
    got_a = shift(parts[2, :cut].astype(jnp.bfloat16), axis, 1)
    got_b = shift(parts[2, cut:].astype(jnp.bfloat16), axis, -1)
    to_right = jnp.concatenate([parts[1, :cut] + got_a.astype(jnp.float32), parts[1, cut:]], axis=0)
    to_left = jnp.concatenate([parts[3, :cut], parts[3, cut:] + got_b.astype(jnp.float32)], axis=0)
    from_left = shift(to_right.astype(jnp.bfloat16), axis, 1)
    from_right = shift(to_left.astype(jnp.bfloat16), axis, -1)
    return parts[0] + from_left.astype(jnp.float32) + from_right.astype(jnp.float32)


def expert_rows(rows, me, width, w_in, w_out):
    half = w_out.shape[0]
    count = SIDE * SIDE
    experts = jnp.arange(count, dtype=jnp.int32)
    high = rows[:, width:width + count].astype(jnp.float32)
    low = rows[:, width + count:width + 2 * count].astype(jnp.float32)
    mine = jnp.sum(jnp.where(experts[None, :] == me, high + low, jnp.float32(0.0)), axis=1)
    projected = jnp.dot(rows[:, :width], w_in, preferred_element_type=jnp.float32)
    inner = (jax.nn.silu(projected[:, :half]) * projected[:, half:]).astype(jnp.bfloat16)
    produced = jnp.dot(inner, w_out, preferred_element_type=jnp.float32).astype(jnp.bfloat16)
    return mine[:, None] * produced.astype(jnp.float32)


def body(hidden_in, route_ids, gates, w_in, w_out):
    assert lax.axis_size("expert") == SIDE * SIDE
    me = lax.axis_index("expert")
    count, width = hidden_in.shape
    experts = jnp.arange(SIDE * SIDE, dtype=jnp.int32)
    table = jnp.sum(
        jnp.where(route_ids[:, :, None] == experts, gates[:, :, None], jnp.float32(0.0)), axis=1
    )
    high = table.astype(jnp.bfloat16)
    low = (table - high.astype(jnp.float32)).astype(jnp.bfloat16)
    extra = jnp.zeros((count, PAD - 2 * SIDE * SIDE), jnp.bfloat16)
    payload = jnp.concatenate([hidden_in, high, low, extra], axis=1)
    rows = gather_ring(gather_ring(payload, 0), 1)
    weighted = expert_rows(rows, me, width, w_in[0], w_out[0])
    part = weighted.reshape(SIDE, SIDE * count, width)
    stage = scatter_ring(part, 1).reshape(SIDE, count, width)
    return scatter_ring(stage, 0).astype(jnp.bfloat16)


def solution(mesh):
    placed = (
        P(("dp", "expert"), None),
        P(("dp", "expert"), None),
        P(("dp", "expert"), None),
        P("expert", None, None),
        P("expert", None, None),
    )
    return jax.shard_map(
        body, mesh=mesh, in_specs=placed, out_specs=P(("dp", "expert"), None), check_vma=False
    )
```

```python
import jax
import jax.numpy as jnp
from jax import lax
from jax.sharding import PartitionSpec as P

SIDE = 4
PAD = 128


def shift(tree, stage, step):
    parts = lax.axis_size("dp")
    pairs = []
    for d in range(parts):
        along_x = (d + stage) % 2 == 0
        for x in range(SIDE):
            for y in range(SIDE):
                if along_x:
                    target = ((x + step) % SIDE) * SIDE + y
                else:
                    target = x * SIDE + (y + step) % SIDE
                pairs.append((d * SIDE * SIDE + x * SIDE + y, d * SIDE * SIDE + target))
    return lax.ppermute(tree, ("dp", "expert"), pairs)


def gather_ring(tree, axis):
    right = shift(tree, axis, -1)
    left = shift(tree, axis, 1)
    cut = jax.tree.leaves(tree)[0].shape[0] // 2
    far_a = shift(jax.tree.map(lambda v: v[:cut], left), axis, 1)
    far_b = shift(jax.tree.map(lambda v: v[cut:], right), axis, -1)
    far = jax.tree.map(lambda a, b: jnp.concatenate([a, b], axis=0), far_a, far_b)
    return jax.tree.map(lambda *vs: jnp.concatenate(vs, axis=0), tree, right, far, left)


def scatter_ring(own, right, far_a, far_b, left, axis):
    got_a = shift(far_a.astype(jnp.bfloat16), axis, 1)
    got_b = shift(far_b.astype(jnp.bfloat16), axis, -1)
    cut = far_a.shape[0]
    to_right = jnp.concatenate([right[:cut] + got_a.astype(jnp.float32), right[cut:]], axis=0)
    to_left = jnp.concatenate([left[:cut], left[cut:] + got_b.astype(jnp.float32)], axis=0)
    from_left = shift(to_right.astype(jnp.bfloat16), axis, 1)
    from_right = shift(to_left.astype(jnp.bfloat16), axis, -1)
    return own + from_left.astype(jnp.float32) + from_right.astype(jnp.float32)


def split_four(block):
    n = block.shape[0] // SIDE
    cut = n // 2
    return block[:n], block[n:2 * n], block[2 * n:2 * n + cut], block[2 * n + cut:3 * n], block[3 * n:]


def expert_rows(rows, me, width, w_in, w_out):
    half = w_out.shape[0]
    count = SIDE * SIDE
    experts = jnp.arange(count, dtype=jnp.int32)
    high = rows[:, width:width + count].astype(jnp.float32)
    low = rows[:, width + count:width + 2 * count].astype(jnp.float32)
    mine = jnp.sum(jnp.where(experts[None, :] == me, high + low, jnp.float32(0.0)), axis=1)
    projected = jnp.dot(rows[:, :width], w_in, preferred_element_type=jnp.float32)
    inner = (jax.nn.silu(projected[:, :half]) * projected[:, half:]).astype(jnp.bfloat16)
    produced = jnp.dot(inner, w_out, preferred_element_type=jnp.float32).astype(jnp.bfloat16)
    return mine[:, None] * produced.astype(jnp.float32)


def body(hidden_in, route_ids, gates, w_in, w_out):
    assert lax.axis_size("expert") == SIDE * SIDE
    me = lax.axis_index("expert")
    count, width = hidden_in.shape
    experts = jnp.arange(SIDE * SIDE, dtype=jnp.int32)
    table = jnp.sum(
        jnp.where(route_ids[:, :, None] == experts, gates[:, :, None], jnp.float32(0.0)), axis=1
    )
    high = table.astype(jnp.bfloat16)
    low = (table - high.astype(jnp.float32)).astype(jnp.bfloat16)
    extra = jnp.zeros((count, PAD - 2 * SIDE * SIDE), jnp.bfloat16)
    payload = jnp.concatenate([hidden_in, high, low, extra], axis=1)
    first = gather_ring(payload, 0)
    right = shift(first, 1, -1)
    left = shift(first, 1, 1)
    cut = first.shape[0] // 2
    far_a = shift(left[:cut], 1, 1)
    far_b = shift(right[cut:], 1, -1)
    pieces = [expert_rows(p, me, width, w_in[0], w_out[0]) for p in (first, right, far_a, far_b, left)]
    stage = scatter_ring(*pieces, 1)
    return scatter_ring(*split_four(stage), 0).astype(jnp.bfloat16)


def solution(mesh):
    placed = (
        P(("dp", "expert"), None),
        P(("dp", "expert"), None),
        P(("dp", "expert"), None),
        P("expert", None, None),
        P("expert", None, None),
    )
    return jax.shard_map(
        body, mesh=mesh, in_specs=placed, out_specs=P(("dp", "expert"), None), check_vma=False
    )
```

```python
import jax
import jax.numpy as jnp
from jax import lax
from jax.sharding import PartitionSpec as P

SIDE = 4
PAD = 128


def shift(tree, stage, step):
    parts = lax.axis_size("dp")
    pairs = []
    for d in range(parts):
        along_x = (d + stage) % 2 == 0
        for x in range(SIDE):
            for y in range(SIDE):
                if along_x:
                    target = ((x + step) % SIDE) * SIDE + y
                else:
                    target = x * SIDE + (y + step) % SIDE
                pairs.append((d * SIDE * SIDE + x * SIDE + y, d * SIDE * SIDE + target))
    return lax.ppermute(tree, ("dp", "expert"), pairs)


def gather_ring(tree, axis):
    right = shift(tree, axis, -1)
    left = shift(tree, axis, 1)
    cut = jax.tree.leaves(tree)[0].shape[0] // 2
    far_a = shift(jax.tree.map(lambda v: v[:cut], left), axis, 1)
    far_b = shift(jax.tree.map(lambda v: v[cut:], right), axis, -1)
    far = jax.tree.map(lambda a, b: jnp.concatenate([a, b], axis=0), far_a, far_b)
    return jax.tree.map(lambda *vs: jnp.concatenate(vs, axis=0), tree, right, far, left)


def scatter_ring(own, right, far_a, far_b, left, axis):
    got_a = shift(far_a.astype(jnp.bfloat16), axis, 1)
    got_b = shift(far_b.astype(jnp.bfloat16), axis, -1)
    cut = far_a.shape[0]
    to_right = jnp.concatenate([right[:cut] + got_a.astype(jnp.float32), right[cut:]], axis=0)
    to_left = jnp.concatenate([left[:cut], left[cut:] + got_b.astype(jnp.float32)], axis=0)
    from_left = shift(to_right.astype(jnp.bfloat16), axis, 1)
    from_right = shift(to_left.astype(jnp.bfloat16), axis, -1)
    return own + from_left.astype(jnp.float32) + from_right.astype(jnp.float32)


def split_four(block):
    n = block.shape[0] // SIDE
    cut = n // 2
    return block[:n], block[n:2 * n], block[2 * n:2 * n + cut], block[2 * n + cut:3 * n], block[3 * n:]


def gate_column(rows, me, width):
    count = SIDE * SIDE
    experts = jnp.arange(count, dtype=jnp.int32)
    high = rows[:, width:width + count].astype(jnp.float32)
    low = rows[:, width + count:width + 2 * count].astype(jnp.float32)
    return jnp.sum(jnp.where(experts[None, :] == me, high + low, jnp.float32(0.0)), axis=1)


def expert_rows(rows, me, width, w_in, w_out, mine=None):
    half = w_out.shape[0]
    if mine is None:
        mine = gate_column(rows, me, width)
    projected = jnp.dot(rows[:, :width], w_in, preferred_element_type=jnp.float32)
    inner = (jax.nn.silu(projected[:, :half]) * projected[:, half:]).astype(jnp.bfloat16)
    produced = jnp.dot(inner, w_out, preferred_element_type=jnp.float32).astype(jnp.bfloat16)
    return mine[:, None] * produced.astype(jnp.float32)


def layer(hidden_in, route_ids, gates, w_in, w_out):
    assert lax.axis_size("expert") == SIDE * SIDE
    me = lax.axis_index("expert")
    count, width = hidden_in.shape
    experts = jnp.arange(SIDE * SIDE, dtype=jnp.int32)
    table = jnp.sum(
        jnp.where(route_ids[:, :, None] == experts, gates[:, :, None], jnp.float32(0.0)), axis=1
    )
    high = table.astype(jnp.bfloat16)
    low = (table - high.astype(jnp.float32)).astype(jnp.bfloat16)
    extra = jnp.zeros((count, PAD - 2 * SIDE * SIDE), jnp.bfloat16)
    payload = jnp.concatenate([hidden_in, high, low, extra], axis=1)
    first = gather_ring(payload, 0)
    first, mine_first = lax.optimization_barrier((first, gate_column(first, me, width)))
    right = shift(first, 1, -1)
    left = shift(first, 1, 1)
    cut = first.shape[0] // 2
    far_a = shift(left[:cut], 1, 1)
    far_b = shift(right[cut:], 1, -1)
    pieces = [expert_rows(first, me, width, w_in[0], w_out[0], mine_first)]
    pieces += [expert_rows(p, me, width, w_in[0], w_out[0]) for p in (right, far_a, far_b, left)]
    stage = scatter_ring(*pieces, 1)
    return scatter_ring(*split_four(stage), 0).astype(jnp.bfloat16)


def solution(mesh):
    placed = (
        P(("dp", "expert"), None),
        P(("dp", "expert"), None),
        P(("dp", "expert"), None),
        P("expert", None, None),
        P("expert", None, None),
    )
    return jax.shard_map(
        layer, mesh=mesh, in_specs=placed, out_specs=P(("dp", "expert"), None), check_vma=False
    )
```

```python
import jax
import jax.numpy as jnp
from jax import lax
from jax.sharding import PartitionSpec as P

SIDE = 4
PAD = 128


def shift(tree, stage, step):
    parts = lax.axis_size("dp")
    pairs = []
    for d in range(parts):
        along_x = (d + stage) % 2 == 0
        for x in range(SIDE):
            for y in range(SIDE):
                if along_x:
                    target = ((x + step) % SIDE) * SIDE + y
                else:
                    target = x * SIDE + (y + step) % SIDE
                pairs.append((d * SIDE * SIDE + x * SIDE + y, d * SIDE * SIDE + target))
    return lax.ppermute(tree, ("dp", "expert"), pairs)


def scatter_ring(own, right, far_a, far_b, left, axis):
    got_a = shift(far_a.astype(jnp.bfloat16), axis, 1)
    got_b = shift(far_b.astype(jnp.bfloat16), axis, -1)
    cut = far_a.shape[0]
    to_right = jnp.concatenate([right[:cut] + got_a.astype(jnp.float32), right[cut:]], axis=0)
    to_left = jnp.concatenate([left[:cut], left[cut:] + got_b.astype(jnp.float32)], axis=0)
    from_left = shift(to_right.astype(jnp.bfloat16), axis, 1)
    from_right = shift(to_left.astype(jnp.bfloat16), axis, -1)
    return own + from_left.astype(jnp.float32) + from_right.astype(jnp.float32)


def gather_direct(block, stage):
    right = shift(block, stage, -1)
    far = shift(block, stage, 2)
    left = shift(block, stage, 1)
    return jnp.concatenate([block, right, far, left], axis=0)


def scatter_direct(parts, stage):
    from_left = shift(parts[1].astype(jnp.bfloat16), stage, 1)
    from_far = shift(parts[2].astype(jnp.bfloat16), stage, 2)
    from_right = shift(parts[3].astype(jnp.bfloat16), stage, -1)
    return parts[0] + from_left.astype(jnp.float32) + from_far.astype(jnp.float32) + from_right.astype(jnp.float32)


def gate_column(rows, me, width):
    count = SIDE * SIDE
    experts = jnp.arange(count, dtype=jnp.int32)
    high = rows[:, width:width + count].astype(jnp.float32)
    low = rows[:, width + count:width + 2 * count].astype(jnp.float32)
    return jnp.sum(jnp.where(experts[None, :] == me, high + low, jnp.float32(0.0)), axis=1)


def expert_rows(rows, me, width, w_in, w_out, mine=None):
    half = w_out.shape[0]
    if mine is None:
        mine = gate_column(rows, me, width)
    projected = jnp.dot(rows[:, :width], w_in, preferred_element_type=jnp.float32)
    inner = (jax.nn.silu(projected[:, :half]) * projected[:, half:]).astype(jnp.bfloat16)
    produced = jnp.dot(inner, w_out, preferred_element_type=jnp.float32).astype(jnp.bfloat16)
    return mine[:, None] * produced.astype(jnp.float32)


def layer(hidden_in, route_ids, gates, w_in, w_out):
    assert lax.axis_size("expert") == SIDE * SIDE
    me = lax.axis_index("expert")
    count, width = hidden_in.shape
    experts = jnp.arange(SIDE * SIDE, dtype=jnp.int32)
    table = jnp.sum(
        jnp.where(route_ids[:, :, None] == experts, gates[:, :, None], jnp.float32(0.0)), axis=1
    )
    high = table.astype(jnp.bfloat16)
    low = (table - high.astype(jnp.float32)).astype(jnp.bfloat16)
    extra = jnp.zeros((count, PAD - 2 * SIDE * SIDE), jnp.bfloat16)
    payload = jnp.concatenate([hidden_in, high, low, extra], axis=1)
    first = gather_direct(payload, 0)
    first, mine_first = lax.optimization_barrier((first, gate_column(first, me, width)))
    right = shift(first, 1, -1)
    left = shift(first, 1, 1)
    cut = first.shape[0] // 2
    far_a = shift(left[:cut], 1, 1)
    far_b = shift(right[cut:], 1, -1)
    pieces = [expert_rows(first, me, width, w_in[0], w_out[0], mine_first)]
    pieces += [expert_rows(p, me, width, w_in[0], w_out[0]) for p in (right, far_a, far_b, left)]
    stage = scatter_ring(*pieces, 1)
    return scatter_direct(stage.reshape(SIDE, count, width), 0).astype(jnp.bfloat16)


def solution(mesh):
    placed = (
        P(("dp", "expert"), None),
        P(("dp", "expert"), None),
        P(("dp", "expert"), None),
        P("expert", None, None),
        P("expert", None, None),
    )
    return jax.shard_map(
        layer, mesh=mesh, in_specs=placed, out_specs=P(("dp", "expert"), None), check_vma=False
    )
```

```python
import jax
import jax.numpy as jnp
from jax import lax
from jax.sharding import PartitionSpec as P

SIDE = 4
PAD = 128


def shift(tree, stage, step):
    parts = lax.axis_size("dp")
    pairs = []
    for d in range(parts):
        along_x = (d + stage) % 2 == 0
        for x in range(SIDE):
            for y in range(SIDE):
                if along_x:
                    target = ((x + step) % SIDE) * SIDE + y
                else:
                    target = x * SIDE + (y + step) % SIDE
                pairs.append((d * SIDE * SIDE + x * SIDE + y, d * SIDE * SIDE + target))
    return lax.ppermute(tree, ("dp", "expert"), pairs)


def scatter_ring(own, right, far_a, far_b, left, axis):
    cut = far_a.shape[0]
    got_a = shift(far_a.astype(jnp.bfloat16), axis, 1)
    got_b = shift(far_b.astype(jnp.bfloat16), axis, -1)
    right_early = shift(right[cut:].astype(jnp.bfloat16), axis, 1)
    left_early = shift(left[:cut].astype(jnp.bfloat16), axis, -1)
    right_late = shift((right[:cut] + got_a.astype(jnp.float32)).astype(jnp.bfloat16), axis, 1)
    left_late = shift((left[cut:] + got_b.astype(jnp.float32)).astype(jnp.bfloat16), axis, -1)
    from_left = jnp.concatenate([right_late, right_early], axis=0).astype(jnp.float32)
    from_right = jnp.concatenate([left_early, left_late], axis=0).astype(jnp.float32)
    return own + from_left + from_right


def gather_direct(block, stage):
    right = shift(block, stage, -1)
    far = shift(block, stage, 2)
    left = shift(block, stage, 1)
    return jnp.concatenate([block, right, far, left], axis=0)


def scatter_direct(parts, stage):
    from_left = shift(parts[1].astype(jnp.bfloat16), stage, 1)
    from_far = shift(parts[2].astype(jnp.bfloat16), stage, 2)
    from_right = shift(parts[3].astype(jnp.bfloat16), stage, -1)
    return parts[0] + from_left.astype(jnp.float32) + from_far.astype(jnp.float32) + from_right.astype(jnp.float32)


def gate_column(rows, me, width):
    count = SIDE * SIDE
    experts = jnp.arange(count, dtype=jnp.int32)
    high = rows[:, width:width + count].astype(jnp.float32)
    low = rows[:, width + count:width + 2 * count].astype(jnp.float32)
    return jnp.sum(jnp.where(experts[None, :] == me, high + low, jnp.float32(0.0)), axis=1)


def expert_rows(rows, me, width, w_in, w_out, mine=None):
    half = w_out.shape[0]
    if mine is None:
        mine = gate_column(rows, me, width)
    projected = jnp.dot(rows[:, :width], w_in, preferred_element_type=jnp.float32)
    inner = (jax.nn.silu(projected[:, :half]) * projected[:, half:]).astype(jnp.bfloat16)
    produced = jnp.dot(inner, w_out, preferred_element_type=jnp.float32).astype(jnp.bfloat16)
    return mine[:, None] * produced.astype(jnp.float32)


def layer(hidden_in, route_ids, gates, w_in, w_out):
    assert lax.axis_size("expert") == SIDE * SIDE
    me = lax.axis_index("expert")
    count, width = hidden_in.shape
    experts = jnp.arange(SIDE * SIDE, dtype=jnp.int32)
    table = jnp.sum(
        jnp.where(route_ids[:, :, None] == experts, gates[:, :, None], jnp.float32(0.0)), axis=1
    )
    high = table.astype(jnp.bfloat16)
    low = (table - high.astype(jnp.float32)).astype(jnp.bfloat16)
    extra = jnp.zeros((count, PAD - 2 * SIDE * SIDE), jnp.bfloat16)
    payload = jnp.concatenate([hidden_in, high, low, extra], axis=1)
    first = gather_direct(payload, 0)
    first, mine_first = lax.optimization_barrier((first, gate_column(first, me, width)))
    cut = first.shape[0] // 2
    right_a = shift(first[:cut], 1, -1)
    right_b = shift(first[cut:], 1, -1)
    left_a = shift(first[:cut], 1, 1)
    left_b = shift(first[cut:], 1, 1)
    far_a = shift(left_a, 1, 1)
    far_b = shift(right_b, 1, -1)
    right = jnp.concatenate([right_a, right_b], axis=0)
    left = jnp.concatenate([left_a, left_b], axis=0)
    pieces = [expert_rows(first, me, width, w_in[0], w_out[0], mine_first)]
    pieces += [expert_rows(p, me, width, w_in[0], w_out[0]) for p in (right, far_a, far_b, left)]
    stage = scatter_ring(*pieces, 1)
    return scatter_direct(stage.reshape(SIDE, count, width), 0).astype(jnp.bfloat16)


def solution(mesh):
    placed = (
        P(("dp", "expert"), None),
        P(("dp", "expert"), None),
        P(("dp", "expert"), None),
        P("expert", None, None),
        P("expert", None, None),
    )
    return jax.shard_map(
        layer, mesh=mesh, in_specs=placed, out_specs=P(("dp", "expert"), None), check_vma=False
    )
```

```python
import jax
import jax.numpy as jnp
from jax import lax
from jax.sharding import PartitionSpec as P

SIDE = 4
PAD = 128


def shift(tree, stage, step):
    parts = lax.axis_size("dp")
    pairs = []
    for d in range(parts):
        along_x = (d + stage) % 2 == 0
        for x in range(SIDE):
            for y in range(SIDE):
                if along_x:
                    target = ((x + step) % SIDE) * SIDE + y
                else:
                    target = x * SIDE + (y + step) % SIDE
                pairs.append((d * SIDE * SIDE + x * SIDE + y, d * SIDE * SIDE + target))
    return lax.ppermute(tree, ("dp", "expert"), pairs)


def scatter_ring(own, right, far_a, far_b, left, axis):
    cut = far_a.shape[0]
    got_a = shift_two(far_a.astype(jnp.bfloat16), axis, 1)
    got_b = shift_two(far_b.astype(jnp.bfloat16), axis, -1)
    right_early = shift(right[cut:].astype(jnp.bfloat16), axis, 1)
    left_early = shift(left[:cut].astype(jnp.bfloat16), axis, -1)
    right_late = shift((right[:cut] + got_a.astype(jnp.float32)).astype(jnp.bfloat16), axis, 1)
    left_late = shift((left[cut:] + got_b.astype(jnp.float32)).astype(jnp.bfloat16), axis, -1)
    from_left = jnp.concatenate([right_late, right_early], axis=0).astype(jnp.float32)
    from_right = jnp.concatenate([left_early, left_late], axis=0).astype(jnp.float32)
    return own + from_left + from_right


def shift_two(block, stage, step):
    cut = block.shape[0] // 2
    return jnp.concatenate([shift(block[:cut], stage, step), shift(block[cut:], stage, step)], axis=0)


def scatter_direct(parts, stage):
    from_left = shift(parts[1].astype(jnp.bfloat16), stage, 1)
    from_far = shift(parts[2].astype(jnp.bfloat16), stage, 2)
    from_right = shift(parts[3].astype(jnp.bfloat16), stage, -1)
    return parts[0] + from_left.astype(jnp.float32) + from_far.astype(jnp.float32) + from_right.astype(jnp.float32)


def gate_column(rows, me, width):
    count = SIDE * SIDE
    experts = jnp.arange(count, dtype=jnp.int32)
    high = rows[:, width:width + count].astype(jnp.float32)
    low = rows[:, width + count:width + 2 * count].astype(jnp.float32)
    return jnp.sum(jnp.where(experts[None, :] == me, high + low, jnp.float32(0.0)), axis=1)


def gate_column_dot(rows, me, width):
    count = SIDE * SIDE
    pick = (jnp.arange(count, dtype=jnp.int32) == me).astype(jnp.float32)
    high = rows[:, width:width + count].astype(jnp.float32)
    low = rows[:, width + count:width + 2 * count].astype(jnp.float32)
    return jnp.dot(high + low, pick, precision=lax.Precision.HIGHEST)


def expert_rows(rows, me, width, w_in, w_out, mine=None):
    half = w_out.shape[0]
    if mine is None:
        mine = gate_column(rows, me, width)
    projected = jnp.dot(rows[:, :width], w_in, preferred_element_type=jnp.float32)
    inner = (jax.nn.silu(projected[:, :half]) * projected[:, half:]).astype(jnp.bfloat16)
    produced = jnp.dot(inner, w_out, preferred_element_type=jnp.float32).astype(jnp.bfloat16)
    return mine[:, None] * produced.astype(jnp.float32)


def layer(hidden_in, route_ids, gates, w_in, w_out):
    assert lax.axis_size("expert") == SIDE * SIDE
    me = lax.axis_index("expert")
    count, width = hidden_in.shape
    experts = jnp.arange(SIDE * SIDE, dtype=jnp.int32)
    table = jnp.sum(
        jnp.where(route_ids[:, :, None] == experts, gates[:, :, None], jnp.float32(0.0)), axis=1
    )
    high = table.astype(jnp.bfloat16)
    low = (table - high.astype(jnp.float32)).astype(jnp.bfloat16)
    extra = jnp.zeros((count, PAD - 2 * SIDE * SIDE), jnp.bfloat16)
    payload = jnp.concatenate([hidden_in, high, low, extra], axis=1)
    right_one = shift(payload, 0, -1)
    far_one = shift(payload, 0, 2)
    left_one = shift(payload, 0, 1)
    first_a = jnp.concatenate([payload, right_one], axis=0)
    first_b = jnp.concatenate([far_one, left_one], axis=0)
    first_a, mine_a = lax.optimization_barrier((first_a, gate_column(first_a, me, width)))
    first_b, mine_b = lax.optimization_barrier((first_b, gate_column_dot(first_b, me, width)))
    right_a = shift(first_a, 1, -1)
    right_b = shift(first_b, 1, -1)
    left_a = shift(first_a, 1, 1)
    left_b = shift(first_b, 1, 1)
    far_a = shift(left_a, 1, 1)
    far_b = shift(right_b, 1, -1)
    right = jnp.concatenate([right_a, right_b], axis=0)
    left = jnp.concatenate([left_a, left_b], axis=0)
    own_a = expert_rows(first_a, me, width, w_in[0], w_out[0], mine_a)
    own_b = expert_rows(first_b, me, width, w_in[0], w_out[0], mine_b)
    pieces = [jnp.concatenate([own_a, own_b], axis=0)]
    pieces += [expert_rows(p, me, width, w_in[0], w_out[0]) for p in (right, far_a, far_b, left)]
    stage = scatter_ring(*pieces, 1)
    return scatter_direct(stage.reshape(SIDE, count, width), 0).astype(jnp.bfloat16)


def solution(mesh):
    placed = (
        P(("dp", "expert"), None),
        P(("dp", "expert"), None),
        P(("dp", "expert"), None),
        P("expert", None, None),
        P("expert", None, None),
    )
    return jax.shard_map(layer, mesh=mesh, in_specs=placed, out_specs=P(("dp", "expert"), None), check_vma=False)
```

```python
import jax
import jax.numpy as jnp
from jax import lax
from jax.sharding import PartitionSpec as P

SIDE = 4
PAD = 128


def shift(tree, stage, step):
    parts = lax.axis_size("dp")
    pairs = []
    for d in range(parts):
        along_x = (d + stage) % 2 == 0
        for x in range(SIDE):
            for y in range(SIDE):
                if along_x:
                    target = ((x + step) % SIDE) * SIDE + y
                else:
                    target = x * SIDE + (y + step) % SIDE
                pairs.append((d * SIDE * SIDE + x * SIDE + y, d * SIDE * SIDE + target))
    return lax.ppermute(tree, ("dp", "expert"), pairs)


def scatter_ring(own, right, far_a, far_b, left, axis):
    cut = far_a.shape[0]
    got_a = shift(far_a.astype(jnp.bfloat16), axis, 1)
    got_b = shift(far_b.astype(jnp.bfloat16), axis, -1)
    right_early = shift(right[cut:].astype(jnp.bfloat16), axis, 1)
    left_early = shift(left[:cut].astype(jnp.bfloat16), axis, -1)
    right_late = shift((right[:cut] + got_a.astype(jnp.float32)).astype(jnp.bfloat16), axis, 1)
    left_late = shift((left[cut:] + got_b.astype(jnp.float32)).astype(jnp.bfloat16), axis, -1)
    from_left = jnp.concatenate([right_late, right_early], axis=0).astype(jnp.float32)
    from_right = jnp.concatenate([left_early, left_late], axis=0).astype(jnp.float32)
    return own + from_left + from_right


def scatter_direct(parts, stage):
    from_left = shift(parts[1].astype(jnp.bfloat16), stage, 1)
    from_far = shift(parts[2].astype(jnp.bfloat16), stage, 2)
    from_right = shift(parts[3].astype(jnp.bfloat16), stage, -1)
    return parts[0] + from_left.astype(jnp.float32) + from_far.astype(jnp.float32) + from_right.astype(jnp.float32)


def gate_column(rows, me, width):
    count = SIDE * SIDE
    experts = jnp.arange(count, dtype=jnp.int32)
    high = rows[:, width:width + count].astype(jnp.float32)
    low = rows[:, width + count:width + 2 * count].astype(jnp.float32)
    return jnp.sum(jnp.where(experts[None, :] == me, high + low, jnp.float32(0.0)), axis=1)


def gate_column_dot(rows, me, width):
    count = SIDE * SIDE
    pick = (jnp.arange(count, dtype=jnp.int32) == me).astype(jnp.float32)
    high = rows[:, width:width + count].astype(jnp.float32)
    low = rows[:, width + count:width + 2 * count].astype(jnp.float32)
    return jnp.dot(high + low, pick, precision=lax.Precision.HIGHEST)


def expert_rows(rows, me, width, w_in, w_out, mine=None):
    half = w_out.shape[0]
    if mine is None:
        mine = gate_column(rows, me, width)
    projected = jnp.dot(rows[:, :width], w_in, preferred_element_type=jnp.float32)
    inner = (jax.nn.silu(projected[:, :half]) * projected[:, half:]).astype(jnp.bfloat16)
    produced = jnp.dot(inner, w_out, preferred_element_type=jnp.float32).astype(jnp.bfloat16)
    return mine[:, None] * produced.astype(jnp.float32)


def layer(hidden_in, route_ids, gates, w_in, w_out):
    assert lax.axis_size("expert") == SIDE * SIDE
    me = lax.axis_index("expert")
    count, width = hidden_in.shape
    experts = jnp.arange(SIDE * SIDE, dtype=jnp.int32)
    table = jnp.sum(
        jnp.where(route_ids[:, :, None] == experts, gates[:, :, None], jnp.float32(0.0)), axis=1
    )
    high = table.astype(jnp.bfloat16)
    low = (table - high.astype(jnp.float32)).astype(jnp.bfloat16)
    extra = jnp.zeros((count, PAD - 2 * SIDE * SIDE), jnp.bfloat16)
    payload = jnp.concatenate([hidden_in, high, low, extra], axis=1)
    right_one = shift(payload, 0, -1)
    far_one = shift(payload, 0, 2)
    left_one = shift(payload, 0, 1)
    first_a = jnp.concatenate([payload, right_one], axis=0)
    first_b = jnp.concatenate([far_one, left_one], axis=0)
    first_a, mine_a = lax.optimization_barrier((first_a, gate_column(first_a, me, width)))
    first_b, mine_b = lax.optimization_barrier((first_b, gate_column_dot(first_b, me, width)))
    right_a = shift(first_a, 1, -1)
    right_b = shift(first_b, 1, -1)
    left_a = shift(first_a, 1, 1)
    left_b = shift(first_b, 1, 1)
    far_a = shift(left_a, 1, 1)
    far_b = shift(right_b, 1, -1)
    right = jnp.concatenate([right_a, right_b], axis=0)
    left = jnp.concatenate([left_a, left_b], axis=0)
    own_a = expert_rows(first_a, me, width, w_in[0], w_out[0], mine_a)
    own_b = expert_rows(first_b, me, width, w_in[0], w_out[0], mine_b)
    pieces = [jnp.concatenate([own_a, own_b], axis=0)]
    cut = far_a.shape[0]
    far = expert_rows(jnp.concatenate([far_a, far_b], axis=0), me, width, w_in[0], w_out[0])
    pieces += [expert_rows(right, me, width, w_in[0], w_out[0]), far[:cut], far[cut:]]
    pieces += [expert_rows(left, me, width, w_in[0], w_out[0])]
    stage = scatter_ring(*pieces, 1)
    return scatter_direct(stage.reshape(SIDE, count, width), 0).astype(jnp.bfloat16)


def solution(mesh):
    placed = (
        P(("dp", "expert"), None),
        P(("dp", "expert"), None),
        P(("dp", "expert"), None),
        P("expert", None, None),
        P("expert", None, None),
    )
    return jax.shard_map(
        layer, mesh=mesh, in_specs=placed, out_specs=P(("dp", "expert"), None), check_vma=False
    )
```

```python
import jax
import jax.numpy as jnp
from jax import lax
from jax.sharding import PartitionSpec as P

SIDE = 4
PAD = 128


def shift(tree, stage, step):
    parts = lax.axis_size("dp")
    pairs = []
    for d in range(parts):
        along_x = (d + stage) % 2 == 0
        for x in range(SIDE):
            for y in range(SIDE):
                if along_x:
                    target = ((x + step) % SIDE) * SIDE + y
                else:
                    target = x * SIDE + (y + step) % SIDE
                pairs.append((d * SIDE * SIDE + x * SIDE + y, d * SIDE * SIDE + target))
    return lax.ppermute(tree, ("dp", "expert"), pairs)


def scatter_ring(own, right, far_a, far_b, left, axis):
    cut = far_a.shape[0]
    got_a = shift(far_a.astype(jnp.bfloat16), axis, 1)
    got_b = shift(far_b.astype(jnp.bfloat16), axis, -1)
    right_early = shift(right[cut:].astype(jnp.bfloat16), axis, 1)
    left_early = shift(left[:cut].astype(jnp.bfloat16), axis, -1)
    right_late = shift((right[:cut] + got_a.astype(jnp.float32)).astype(jnp.bfloat16), axis, 1)
    left_late = shift((left[cut:] + got_b.astype(jnp.float32)).astype(jnp.bfloat16), axis, -1)
    from_left = jnp.concatenate([right_late, right_early], axis=0).astype(jnp.float32)
    from_right = jnp.concatenate([left_early, left_late], axis=0).astype(jnp.float32)
    return own + from_left + from_right


def scatter_direct(parts, stage):
    from_left = shift(parts[1].astype(jnp.bfloat16), stage, 1)
    from_far = shift(parts[2].astype(jnp.bfloat16), stage, 2)
    from_right = shift(parts[3].astype(jnp.bfloat16), stage, -1)
    return parts[0] + from_left.astype(jnp.float32) + from_far.astype(jnp.float32) + from_right.astype(jnp.float32)


def gate_column(rows, me, width):
    count = SIDE * SIDE
    experts = jnp.arange(count, dtype=jnp.int32)
    high = rows[:, width:width + count].astype(jnp.float32)
    low = rows[:, width + count:width + 2 * count].astype(jnp.float32)
    return jnp.sum(jnp.where(experts[None, :] == me, high + low, jnp.float32(0.0)), axis=1)


def gate_column_dot(rows, me, width):
    count = SIDE * SIDE
    pick = (jnp.arange(count, dtype=jnp.int32) == me).astype(jnp.float32)
    high = rows[:, width:width + count].astype(jnp.float32)
    low = rows[:, width + count:width + 2 * count].astype(jnp.float32)
    return jnp.dot(high + low, pick, precision=lax.Precision.HIGHEST)


def expert_rows(rows, me, width, w_in, w_out, mine=None):
    half = w_out.shape[0]
    if mine is None:
        mine = gate_column(rows, me, width)
    projected = jnp.dot(rows[:, :width], w_in, preferred_element_type=jnp.float32)
    inner = (jax.nn.silu(projected[:, :half]) * projected[:, half:]).astype(jnp.bfloat16)
    produced = jnp.dot(inner, w_out, preferred_element_type=jnp.float32).astype(jnp.bfloat16)
    return mine[:, None] * produced.astype(jnp.float32)


def layer(hidden_in, route_ids, gates, w_in, w_out):
    assert lax.axis_size("expert") == SIDE * SIDE
    me = lax.axis_index("expert")
    count, width = hidden_in.shape
    experts = jnp.arange(SIDE * SIDE, dtype=jnp.int32)
    table = jnp.sum(
        jnp.where(route_ids[:, :, None] == experts, gates[:, :, None], jnp.float32(0.0)), axis=1
    )
    high = table.astype(jnp.bfloat16)
    low = (table - high.astype(jnp.float32)).astype(jnp.bfloat16)
    extra = jnp.zeros((count, PAD - 2 * SIDE * SIDE), jnp.bfloat16)
    payload = jnp.concatenate([hidden_in, high, low, extra], axis=1)
    right_one = shift(payload, 0, -1)
    far_one = shift(payload, 0, 2)
    left_one = shift(payload, 0, 1)
    first_a = jnp.concatenate([payload, right_one], axis=0)
    first_b = jnp.concatenate([far_one, left_one], axis=0)
    first_a, mine_a = lax.optimization_barrier((first_a, gate_column(first_a, me, width)))
    first_b, mine_b = lax.optimization_barrier((first_b, gate_column_dot(first_b, me, width)))
    right_a = shift(first_a, 1, -1)
    right_b = shift(first_b, 1, -1)
    left_a = shift(first_a, 1, 1)
    left_b = shift(first_b, 1, 1)
    far_a = shift(left_a, 1, 1)
    far_b = shift(right_b, 1, -1)
    right = jnp.concatenate([right_a, right_b], axis=0)
    left = jnp.concatenate([left_a, left_b], axis=0)
    own_a = expert_rows(first_a, me, width, w_in[0], w_out[0], mine_a)
    own_b = expert_rows(first_b, me, width, w_in[0], w_out[0], mine_b)
    pieces = [jnp.concatenate([own_a, own_b], axis=0)]
    pieces += [expert_rows(p, me, width, w_in[0], w_out[0]) for p in (right, far_a, far_b, left)]
    stage = scatter_ring(*pieces, 1)
    return scatter_direct(stage.reshape(SIDE, count, width), 0).astype(jnp.bfloat16)


def solution(mesh):
    placed = (
        P(("dp", "expert"), None),
        P(("dp", "expert"), None),
        P(("dp", "expert"), None),
        P("expert", None, None),
        P("expert", None, None),
    )
    return jax.shard_map(layer, mesh=mesh, in_specs=placed, out_specs=P(("dp", "expert"), None), check_vma=False)
```
